256 devices in a mesh: wide: 32 (over z_hi, y, core), narrow: 8 (over z_lo, x).
Axes of the slice: x: 4, y: 4, z: 8 (z_hi: 4, z_lo: 2; z = z_hi * 2 + z_lo), core: 2. Of those that a mesh axis runs over, the one named last changes fastest.
Arguments:
- residual: bfloat16 [256, 8192], P('wide'), may hold values from -60 to 60
- norm_gain: float32 [8192], replicated, may hold values from 0.1 to 1.9
- w_query: bfloat16 [8192, 8192], P('wide', 'narrow'), may hold values from -0.0625 to 0.0625
- key_projection_weight: bfloat16 [8192, 1024], P('wide', 'narrow'), may hold values from -0.0625 to 0.0625
- value_projection_weight: bfloat16 [8192, 1024], P('wide', 'narrow'), may hold values from -0.0625 to 0.0625
- w_out: bfloat16 [8192, 8192], P('narrow', 'wide'), may hold values from -0.5 to 0.5
- cache_keys: bfloat16 [256, 8, 1024, 128], P('wide', 'narrow'), may hold values from -480 to 480
- stored_values: bfloat16 [256, 8, 1024, 128], P('wide', 'narrow'), may hold values from -24 to 24
- lengths: int32 [256], P('wide'), may hold values from 1 to 1024, as said below
- w_enc: bfloat16 [8192, 65536], P('narrow', 'wide'), may hold values from -0.0625 to 0.0625
- b_enc: float32 [65536], P('wide'), may hold values from -3 to 3
- w_dec: bfloat16 [65536, 8192], P('wide', 'narrow'), may hold values from -0.0625 to 0.0625
- b_dec: float32 [8192], P('narrow'), may hold values from -3 to 3
- clamp_index: int32 [256, 8], replicated, may hold values from 0 to 65535, as said below
- clamp_value: float32 [256, 8], replicated, may hold values from 10 to 40
Outputs:
- steered: bfloat16 [256, 8192], P('wide', 'narrow')
The draws below stay inside these ranges and needn't reach their ends.
Inputs may be any that keep to these rules, and one draw needn't show every extreme that they name: `lengths`: row 0 has all 1024 slots filled. `clamp_index`: the 8 latents of a row are distinct.
All inputs are finite; a program needn't handle non-finite values.
Results may differ from the reference program's by a relative error of at most 0.014.
The reference program's roundings to bfloat16 on the way count: a program that leaves them out, or rounds other values in their place, can miss the bound.
Values may be sent and summed in bfloat16 or wider, within the bound.
No kernel may reach another device: no remote copies, remote signals or barrier semaphores. Data moves between devices by JAX's collectives and lax.ppermute only.
A program may use at most 64 MiB of HBM per device.

```python
import math
import jax
import jax.numpy as jnp
from jax import lax

MODEL_WIDTH = 8192
QUERY_HEADS = 64
KEY_VALUE_HEADS = 8
HEAD_WIDTH = 128
LAT = 65536
CLAMPS = 8
CACHE_SLOTS = 1024
DECODED_ROWS = 256


def draw_residual(key, part):
    random_key_first, random_key_second = jax.random.split(key, 2)
    row_scale = jnp.exp(jax.random.uniform(random_key_second, (DECODED_ROWS, 1), jnp.float32, math.log(0.3), math.log(3.0)))
    frequency_base = jnp.clip(jax.random.normal(random_key_first, (DECODED_ROWS, MODEL_WIDTH), jnp.float32), -6.0, 6.0)
    return (frequency_base * row_scale).astype(jnp.bfloat16)


def draw_cache_keys(key, part):
    random_key_first = jax.random.fold_in(key, 0)
    frequency_base = jnp.clip(jax.random.normal(random_key_first, (DECODED_ROWS, KEY_VALUE_HEADS, CACHE_SLOTS, HEAD_WIDTH), jnp.float32), -6.0, 6.0)
    return frequency_base.astype(jnp.bfloat16)


def draw_lengths(key, part):
    filled = jax.random.randint(key, (DECODED_ROWS,), 1, CACHE_SLOTS + 1, dtype=jnp.int32)
    return filled.at[0].set(CACHE_SLOTS)


def draw_clamp_index(key, part):
    span = LAT // CLAMPS
    offsets = jnp.arange(CLAMPS, dtype=jnp.int32) * span
    selected_latents = offsets[None, :] + jax.random.randint(key, (DECODED_ROWS, CLAMPS), 0, span, dtype=jnp.int32)
    selected_latents = selected_latents.at[0, CLAMPS - 1].set(LAT - 1)
    return selected_latents.at[1, 0].set(0)


def steps_of(rng, extent, cuts, low, top_value):
    level, own = 1.0, jax.random.fold_in(rng, 6)
    for dim, shards_of in cuts:
        heights = jnp.exp(jax.random.uniform(jax.random.fold_in(own, dim), (shards_of,), jnp.float32, low / len(cuts), top_value / len(cuts)))
        level = level * jnp.repeat(heights, extent[dim] // shards_of).reshape([-1 if axis == dim else 1 for axis in range(len(extent))])
    return level


def gaussian(stream_key, dims, width, bound, cuts=(), kind=jnp.bfloat16):
    loudness = steps_of(stream_key, dims, cuts, -0.22, 0.18) if cuts else 1.0
    values = jax.random.normal(stream_key, dims, jnp.float32) * width * loudness
    return jnp.minimum(jnp.maximum(values, -bound), bound).astype(kind)


def setup_inputs(seed: int = 0) -> dict:
    key_of = jax.random.split(jax.random.key(seed), 16)
    residual = draw_residual(jax.random.fold_in(key_of[15], 71), 0)
    norm_gain = jnp.clip(1.0 + 0.18 * jax.random.normal(key_of[1], (MODEL_WIDTH,), jnp.float32), 0.1, 1.9)
    w_query = gaussian(key_of[2], (MODEL_WIDTH, QUERY_HEADS * HEAD_WIDTH), MODEL_WIDTH ** -0.5, 0.0625, ((0, 32), (1, 8)))
    key_projection_weight = gaussian(key_of[3], (MODEL_WIDTH, KEY_VALUE_HEADS * HEAD_WIDTH), MODEL_WIDTH ** -0.5, 0.0625, ((0, 32), (1, 8)))
    value_projection_weight = gaussian(key_of[4], (MODEL_WIDTH, KEY_VALUE_HEADS * HEAD_WIDTH), MODEL_WIDTH ** -0.5, 0.0625, ((0, 32), (1, 8)))
    w_out = gaussian(key_of[5], (QUERY_HEADS * HEAD_WIDTH, MODEL_WIDTH), HEAD_WIDTH ** -0.5, 0.5, ((0, 8), (1, 32)))
    cache_keys = draw_cache_keys(jax.random.fold_in(key_of[15], 71), 0)
    stored_values = gaussian(key_of[7], (DECODED_ROWS, KEY_VALUE_HEADS, CACHE_SLOTS, HEAD_WIDTH), 4.0, 24.0, ((0, 32), (1, 8)))
    lengths = draw_lengths(jax.random.fold_in(key_of[15], 71), 0)
    w_enc = gaussian(key_of[9], (MODEL_WIDTH, LAT), MODEL_WIDTH ** -0.5, 0.0625, ((0, 8), (1, 32)))
    b_enc = gaussian(key_of[10], (LAT,), 0.5, 3.0, ((0, 32),), jnp.float32)
    w_dec = gaussian(key_of[11], (LAT, MODEL_WIDTH), MODEL_WIDTH ** -0.5, 0.0625, ((0, 32), (1, 8)))
    b_dec = gaussian(key_of[12], (MODEL_WIDTH,), 0.5, 3.0, ((0, 8),), jnp.float32)
    clamp_index = draw_clamp_index(jax.random.fold_in(key_of[15], 71), 0)
    clamp_value = jnp.clip(jax.random.uniform(key_of[14], (DECODED_ROWS, CLAMPS), jnp.float32, 10.0, 40.0), 10.0, 40.0)
    return dict(residual=residual, norm_gain=norm_gain, w_query=w_query, key_projection_weight=key_projection_weight, value_projection_weight=value_projection_weight, w_out=w_out, cache_keys=cache_keys, stored_values=stored_values, lengths=lengths, w_enc=w_enc, b_enc=b_enc, w_dec=w_dec, b_dec=b_dec, clamp_index=clamp_index, clamp_value=clamp_value)


rope_base = 500000.0

def rotary(vectors, positions):
    halfway = vectors.shape[-1] // 2
    counter = jnp.arange(halfway, dtype=jnp.float32)
    inverse = rope_base ** (-2.0 * counter / vectors.shape[-1])
    angles = positions.astype(jnp.float32)[:, None] * inverse[None, :]
    cosine = jnp.cos(angles)[:, None, :]
    sine = jnp.sin(angles)[:, None, :]
    first_half = vectors[..., :halfway]
    second_half = vectors[..., halfway:]
    return jnp.concatenate([first_half * cosine - second_half * sine, second_half * cosine + first_half * sine], axis=-1)

def clamp_latents(pre_acts, latent_first, clamp_index, clamp_value):
    columns = latent_first + jnp.arange(pre_acts.shape[1], dtype=jnp.int32)
    result = jnp.maximum(pre_acts, 0.0)
    for clamp_slot in range(clamp_index.shape[1]):
        matched = columns[None, :] == clamp_index[:, clamp_slot:clamp_slot + 1]
        result = jnp.where(matched, clamp_value[:, clamp_slot:clamp_slot + 1], result)
    return result.astype(jnp.bfloat16)

def attend_row(packed):
    current_query, key_row, value_row, key_cache, value_cache, length = packed
    query_group_width = QUERY_HEADS // KEY_VALUE_HEADS
    grouped_queries = current_query.astype(jnp.float32).reshape(KEY_VALUE_HEADS, query_group_width, HEAD_WIDTH)
    scaling = 1.0 / math.sqrt(HEAD_WIDTH)
    scores = jnp.einsum('kgd,kjd->kgj', grouped_queries, key_cache.astype(jnp.float32)) * scaling
    in_range = jnp.arange(key_cache.shape[1], dtype=jnp.int32) < length
    scores = jnp.where(in_range[None, None, :], scores, -jnp.inf)
    own_score = jnp.einsum('kgd,kd->kg', grouped_queries, key_row.astype(jnp.float32)) * scaling
    highest = jnp.maximum(lax.optimization_barrier(jnp.max(scores, axis=-1)), own_score)
    weights = jnp.exp(scores - highest[..., None])
    own_weight = jnp.exp(own_score - highest)
    denominator = lax.optimization_barrier(jnp.sum(weights, axis=-1)) + own_weight
    probabilities = (weights / denominator[..., None]).astype(jnp.bfloat16)
    own_prob = (own_weight / denominator).astype(jnp.bfloat16)
    blended = jnp.einsum('kgj,kjd->kgd', probabilities.astype(jnp.float32), value_cache.astype(jnp.float32))
    blended = blended + own_prob.astype(jnp.float32)[..., None] * value_row.astype(jnp.float32)[:, None, :]
    return blended.astype(jnp.bfloat16).reshape(QUERY_HEADS * HEAD_WIDTH)

def reference(residual, norm_gain, w_query, key_projection_weight, value_projection_weight, w_out, cache_keys, stored_values, lengths, w_enc, b_enc, w_dec, b_dec, clamp_index, clamp_value):
    stream = residual.astype(jnp.float32)
    normalized_rows = (stream * lax.rsqrt(lax.optimization_barrier(jnp.mean(stream * stream, axis=-1, keepdims=True)) + 1e-05) * norm_gain[None, :]).astype(jnp.bfloat16)
    query_full = jnp.dot(normalized_rows, w_query, preferred_element_type=jnp.float32).reshape(DECODED_ROWS, QUERY_HEADS, HEAD_WIDTH)
    complete_keys = jnp.dot(normalized_rows, key_projection_weight, preferred_element_type=jnp.float32).reshape(DECODED_ROWS, KEY_VALUE_HEADS, HEAD_WIDTH)
    complete_values = jnp.dot(normalized_rows, value_projection_weight, preferred_element_type=jnp.float32).reshape(DECODED_ROWS, KEY_VALUE_HEADS, HEAD_WIDTH)
    queries = rotary(query_full, lengths).astype(jnp.bfloat16)
    key_new = rotary(complete_keys, lengths).astype(jnp.bfloat16)
    value_new = complete_values.astype(jnp.bfloat16)
    attended = lax.map(attend_row, (queries, key_new, value_new, cache_keys, stored_values, lengths))
    hidden = (stream + jnp.dot(attended, w_out, preferred_element_type=jnp.float32)).astype(jnp.bfloat16)
    pre_acts = jnp.dot(hidden, w_enc, preferred_element_type=jnp.float32) + b_enc[None, :]
    activations = clamp_latents(pre_acts, 0, clamp_index, clamp_value)
    rebuilt = jnp.dot(activations, w_dec, preferred_element_type=jnp.float32)
    return (rebuilt + b_dec[None, :]).astype(jnp.bfloat16)
```

```python
import math

import jax
import jax.numpy as jnp
from jax import lax
from jax.sharding import PartitionSpec as P

HEAD_WIDTH = 128


rope_base = 500000.0


def rotary(vectors, positions):
    halfway = vectors.shape[-1] // 2
    counter = jnp.arange(halfway, dtype=jnp.float32)
    inverse = rope_base ** (-2.0 * counter / vectors.shape[-1])
    angles = positions.astype(jnp.float32)[:, None] * inverse[None, :]
    cosine = jnp.cos(angles)[:, None, :]
    sine = jnp.sin(angles)[:, None, :]
    first_half = vectors[..., :halfway]
    second_half = vectors[..., halfway:]
    return jnp.concatenate(
        [first_half * cosine - second_half * sine, second_half * cosine + first_half * sine],
        axis=-1,
    )


def scatter_sum(partial, axis_name, groups, dim):
    shape = partial.shape
    pieces = partial.reshape(shape[:dim] + (groups, shape[dim] // groups) + shape[dim + 1 :])
    pieces = jnp.moveaxis(pieces, dim, 0)
    moved = lax.all_to_all(pieces, axis_name, split_axis=0, concat_axis=0, tiled=True)
    return jnp.sum(moved, axis=0)


def gather_rows(block, axis_name, groups):
    copies = jnp.broadcast_to(block[None], (groups,) + block.shape)
    moved = lax.all_to_all(copies, axis_name, split_axis=0, concat_axis=0, tiled=True)
    return moved.reshape((groups * block.shape[0],) + block.shape[1:])


def clamp_latents(pre_acts, latent_first, clamp_index, clamp_value):
    columns = latent_first + jnp.arange(pre_acts.shape[1], dtype=jnp.int32)
    result = jnp.maximum(pre_acts, 0.0)
    for clamp_slot in range(clamp_index.shape[1]):
        matched = columns[None, :] == clamp_index[:, clamp_slot : clamp_slot + 1]
        result = jnp.where(matched, clamp_value[:, clamp_slot : clamp_slot + 1], result)
    return result.astype(jnp.bfloat16)


def attend(queries, key_new, value_new, cache_keys, stored_values, lengths):
    local_rows, heads_here, head_size = queries.shape
    kv_here = key_new.shape[1]
    query_group_width = heads_here // kv_here
    grouped_queries = queries.reshape(local_rows, kv_here, query_group_width, head_size)
    scaling = 1.0 / math.sqrt(head_size)
    scores = (
        jnp.einsum(
            "rkgd,rkjd->rkgj", grouped_queries, cache_keys, preferred_element_type=jnp.float32
        )
        * scaling
    )
    in_range = (
        jnp.arange(cache_keys.shape[2], dtype=jnp.int32)[None, None, None, :]
        < lengths[:, None, None, None]
    )
    scores = jnp.where(in_range, scores, -jnp.inf)
    own_score = (
        jnp.einsum("rkgd,rkd->rkg", grouped_queries, key_new, preferred_element_type=jnp.float32)
        * scaling
    )
    highest = jnp.maximum(jnp.max(scores, axis=-1), own_score)
    weights = jnp.exp(scores - highest[..., None])
    own_weight = jnp.exp(own_score - highest)
    denominator = jnp.sum(weights, axis=-1) + own_weight
    probabilities = (weights / denominator[..., None]).astype(jnp.bfloat16)
    own_prob = (own_weight / denominator).astype(jnp.bfloat16)
    blended = jnp.einsum(
        "rkgj,rkjd->rkgd", probabilities, stored_values, preferred_element_type=jnp.float32
    )
    blended = (
        blended
        + own_prob.astype(jnp.float32)[..., None] * value_new.astype(jnp.float32)[:, :, None, :]
    )
    return blended.astype(jnp.bfloat16).reshape(local_rows, heads_here * head_size)


def on_device(
    residual,
    norm_gain,
    w_query,
    key_projection_weight,
    value_projection_weight,
    w_out,
    cache_keys,
    stored_values,
    lengths,
    w_enc,
    b_enc,
    w_dec,
    b_dec,
    clamp_index,
    clamp_value,
):
    stream = residual.astype(jnp.float32)
    local_rows = residual.shape[0]
    normalized_rows = (
        stream
        * lax.rsqrt(jnp.mean(stream * stream, axis=-1, keepdims=True) + 1e-05)
        * norm_gain[None, :]
    ).astype(jnp.bfloat16)
    by_feature = lax.all_to_all(normalized_rows, "wide", split_axis=1, concat_axis=0, tiled=True)
    query_width = w_query.shape[1]
    key_width = key_projection_weight.shape[1]
    row_block = by_feature
    wide_size = lax.axis_size("wide")
    narrow_size = lax.axis_size("narrow")
    projected = scatter_sum(
        jnp.concatenate(
            [
                jnp.dot(row_block, w_query, preferred_element_type=jnp.float32),
                jnp.dot(row_block, key_projection_weight, preferred_element_type=jnp.float32),
                jnp.dot(row_block, value_projection_weight, preferred_element_type=jnp.float32),
            ],
            axis=1,
        ),
        "wide",
        wide_size,
        0,
    )
    heads_here = query_width // HEAD_WIDTH
    kv_here = key_width // HEAD_WIDTH
    queries = rotary(
        projected[:, :query_width].reshape(local_rows, heads_here, HEAD_WIDTH), lengths
    ).astype(jnp.bfloat16)
    key_new = rotary(
        projected[:, query_width : query_width + key_width].reshape(
            local_rows, kv_here, HEAD_WIDTH
        ),
        lengths,
    ).astype(jnp.bfloat16)
    value_new = (
        projected[:, query_width + key_width :]
        .reshape(local_rows, kv_here, HEAD_WIDTH)
        .astype(jnp.bfloat16)
    )
    attended = attend(queries, key_new, value_new, cache_keys, stored_values, lengths)
    partial_out = jnp.dot(
        gather_rows(attended, "wide", wide_size),
        w_out,
        preferred_element_type=jnp.float32,
    )
    by_row = lax.all_to_all(partial_out, "wide", split_axis=0, concat_axis=1, tiled=True)
    head_total = scatter_sum(by_row, "narrow", narrow_size, 1)
    width_here = w_enc.shape[0]
    narrow_index = lax.axis_index("narrow")
    own_stream = lax.dynamic_slice_in_dim(stream, narrow_index * width_here, width_here, 1)
    hidden = (own_stream + head_total).astype(jnp.bfloat16)
    partial_pre = jnp.dot(
        gather_rows(hidden, "wide", wide_size),
        w_enc,
        preferred_element_type=jnp.float32,
    )
    latents_here = w_enc.shape[1]
    latent_first = lax.axis_index("wide") * latents_here
    summed_pre = scatter_sum(partial_pre, "narrow", narrow_size, 0)
    rows_here = summed_pre.shape[0]
    own_clamps = lax.dynamic_slice_in_dim(clamp_index, narrow_index * rows_here, rows_here, 0)
    own_values = lax.dynamic_slice_in_dim(clamp_value, narrow_index * rows_here, rows_here, 0)
    activations = gather_rows(
        clamp_latents(summed_pre + b_enc[None, :], latent_first, own_clamps, own_values),
        "narrow",
        narrow_size,
    )
    row_block = activations
    rebuilt = scatter_sum(
        jnp.dot(row_block, w_dec, preferred_element_type=jnp.float32),
        "wide",
        wide_size,
        0,
    )
    return (rebuilt + b_dec[None, :]).astype(jnp.bfloat16)


def solution(mesh):
    placed = (
        P("wide", None),
        P(),
        P("wide", "narrow"),
        P("wide", "narrow"),
        P("wide", "narrow"),
        P("narrow", "wide"),
        P("wide", "narrow", None, None),
        P("wide", "narrow", None, None),
        P("wide"),
        P("narrow", "wide"),
        P("wide"),
        P("wide", "narrow"),
        P("narrow"),
        P(),
        P(),
    )
    return jax.shard_map(
        on_device, mesh=mesh, in_specs=placed, out_specs=P("wide", "narrow"), check_vma=False
    )
```
